512 devices in a mesh: rep: 32 (over z, core), row: 4 (over x), col: 4 (over y).
Axes of the slice: x: 4, y: 4, z: 16, core: 2. Of those that a mesh axis runs over, the one named last changes fastest.
Arguments:
- coordinates: bfloat16 [128, 32, 3, 128], P('rep')
- resample: int32 [32, 22], P('rep'), may hold values from 0 to 127, as said below
- block_slot: int32 [128], replicated, may hold values from 0 to 127, as said below
- lag_time: int32 [32], P('rep'), may hold values from 1 to 8
- atom_pairs: int32 [2, 4096], replicated, may hold values from 0 to 127, as said below
Outputs:
- instant_cov: bfloat16 [32, 4096, 4096], P('rep', 'row', 'col')
- lagged_cov: bfloat16 [32, 4096, 4096], P('rep', 'row', 'col')
The draws below stay inside these ranges and needn't reach their ends.
Inputs may be any that keep to these rules, and one draw needn't show every extreme that they name: `resample`: the owner of a block is block_slot // 4. In each replicate at most 2 draws have one owner, and some owner has exactly 2; a block may be drawn more than once. `block_slot`: each slot holds exactly one block. `atom_pairs`: the two atoms of a feature differ, and no unordered pair of atoms appears twice.
All inputs are finite; a program needn't handle non-finite values.
Results may differ from the reference program's by a relative error of at most 0.0073.
Values may be sent and summed in bfloat16 or wider, within the bound.
No kernel may reach another device: no remote copies, remote signals or barrier semaphores. Data moves between devices by JAX's collectives and lax.ppermute only.
A program may use at most 64 MiB of HBM per device.

```python
import math
import jax
import jax.numpy as jnp
from jax import lax

F = 4096
ATOMS = 128
BLOCK_LEN = 32
DRAWS = 22
LAG_MAX = 8
BLK_DEV = 4
REPLICATES = 32
BLOCKS = 128
CAP = 2


def slot_order(key):
    return jax.random.permutation(jax.random.fold_in(key, 11), BLOCKS).astype(jnp.int32)


def draw_block_slot(key, part):
    return slot_order(key)


def draw_resample(key, part):
    slot_table = slot_order(key)
    inverse = jnp.argsort(slot_table).astype(jnp.int32)
    owner_total = BLOCKS // BLK_DEV
    item_total = owner_total * CAP

    def one_replicate(replicate):
        sub_key = jax.random.fold_in(jax.random.fold_in(key, 23), replicate)
        sub_keys = jax.random.split(sub_key, 4)
        item_place = jnp.argsort(jax.random.permutation(sub_keys[0], item_total)).astype(jnp.int32)
        first_owner = jax.random.randint(sub_keys[1], (), 0, owner_total)
        item_owner = jnp.arange(item_total, dtype=jnp.int32) % owner_total
        item_score = jnp.where(item_owner == first_owner, item_place - item_total, item_place)
        chosen = jnp.argsort(item_score)[:DRAWS].astype(jnp.int32) % owner_total
        chosen = chosen[jax.random.permutation(sub_keys[3], DRAWS)]
        local_slot = jax.random.randint(sub_keys[2], (DRAWS,), 0, BLK_DEV)
        return inverse[chosen * BLK_DEV + local_slot]
    return jax.vmap(one_replicate)(jnp.arange(REPLICATES, dtype=jnp.int32))


def draw_atom_pairs(key, part):
    chosen = jax.random.permutation(jax.random.fold_in(key, 31), ATOMS * (ATOMS // 2 - 1))[:F].astype(jnp.int32)
    first_atoms = chosen % ATOMS
    offsets = chosen // ATOMS + 1
    second_atoms = (first_atoms + offsets) % ATOMS
    return jnp.stack([first_atoms, second_atoms]).astype(jnp.int32)


def draw_coordinates(key, part):
    sub_keys = jax.random.split(jax.random.fold_in(key, 41), 6)
    full_shape = (BLOCKS, BLOCK_LEN, 3, ATOMS)
    center_pos = 2.0 * jax.random.normal(sub_keys[0], (1, 1, 3, ATOMS), jnp.float32)
    block_scale = jnp.exp(jax.random.uniform(sub_keys[1], (BLOCKS, 1, 1, 1), jnp.float32, math.log(0.5), math.log(2.0)))
    frequency = jax.random.uniform(sub_keys[2], (BLOCKS, 1, 3, ATOMS), jnp.float32, 0.1, 0.9)
    phase_shift = jax.random.uniform(sub_keys[3], (BLOCKS, 1, 3, ATOMS), jnp.float32, -math.pi, math.pi)
    amplitude = jax.random.uniform(sub_keys[4], (1, 1, 3, ATOMS), jnp.float32, 0.5, 1.5)
    frame_time = jnp.arange(BLOCK_LEN, dtype=jnp.float32).reshape(1, BLOCK_LEN, 1, 1)
    jitter = 0.4 * jax.random.normal(sub_keys[5], full_shape, jnp.float32)
    values = center_pos + block_scale * (amplitude * jnp.cos(frequency * frame_time + phase_shift) + jitter)
    return values.astype(jnp.bfloat16)


def place_ends(array, own_key, least, largest):
    longest = array.shape.index(max(array.shape))
    spots = []
    for shift in (0, 1):
        where = [jax.random.randint(jax.random.fold_in(own_key, axis), (), 0, length) for axis, length in enumerate(array.shape)]
        where[longest] = (where[longest] + shift) % array.shape[longest]
        spots.append(tuple(where))
    return array.at[spots[0]].set(least).at[spots[1]].set(largest)


def setup_inputs(seed: int = 0) -> dict:
    key_of = jax.random.split(jax.random.key(seed), 6)
    coordinates = draw_coordinates(jax.random.fold_in(key_of[5], 71), 0)
    resample = draw_resample(jax.random.fold_in(key_of[5], 71), 0)
    block_slot = draw_block_slot(jax.random.fold_in(key_of[5], 71), 0)
    lag_time = place_ends(jax.random.randint(key_of[3], (REPLICATES,), 1, LAG_MAX + 1), jax.random.fold_in(key_of[3], 1), 1, LAG_MAX).astype(jnp.int32)
    atom_pairs = draw_atom_pairs(jax.random.fold_in(key_of[5], 71), 0)
    return {"coordinates": coordinates, "resample": resample, "block_slot": block_slot, "lag_time": lag_time, "atom_pairs": atom_pairs}


def featurize(blocks_xyz, first_atoms, second_atoms):
    positions = blocks_xyz.astype(jnp.float32)
    difference = positions[..., first_atoms] - positions[..., second_atoms]
    squared = difference[:, :, 0] * difference[:, :, 0] + difference[:, :, 1] * difference[:, :, 1] + difference[:, :, 2] * difference[:, :, 2]
    return jnp.sqrt(squared).astype(jnp.bfloat16)

def centered(features, shift):
    width_total = features.shape[-1]
    doubled = jnp.concatenate([features, features], axis=1)
    shifted = lax.dynamic_slice_in_dim(doubled, shift, BLOCK_LEN, axis=1)
    valid_rows = (jnp.arange(BLOCK_LEN, dtype=jnp.int32) < BLOCK_LEN - shift)[None, :, None]
    pair_count = (2 * DRAWS * (BLOCK_LEN - shift)).astype(jnp.float32)
    earlier = jnp.where(valid_rows, features.astype(jnp.float32), 0.0)
    later = jnp.where(valid_rows, shifted.astype(jnp.float32), 0.0)
    feature_mean = (lax.optimization_barrier(jnp.sum(earlier, axis=(0, 1))) + lax.optimization_barrier(jnp.sum(later, axis=(0, 1)))) / pair_count
    zero_lag = jnp.where(valid_rows, earlier - feature_mean, 0.0).astype(jnp.bfloat16).reshape(-1, width_total)
    lagged = jnp.where(valid_rows, later - feature_mean, 0.0).astype(jnp.bfloat16).reshape(-1, width_total)
    return (zero_lag, lagged, pair_count)

def reference(coordinates, resample, block_slot, lag_time, atom_pairs):

    def one_replicate(inputs):
        drawn_blocks, shift = inputs
        slots = block_slot[drawn_blocks]
        selected = coordinates[slots]
        features = featurize(selected, atom_pairs[0], atom_pairs[1])
        zero_lag, lagged, pair_count = centered(features, shift)
        first_part = zero_lag.astype(jnp.float32)
        second_part = lagged.astype(jnp.float32)
        highest = lax.Precision.HIGHEST
        instant = jnp.dot(first_part.T, first_part, precision=highest) + jnp.dot(second_part.T, second_part, precision=highest)
        crossed = jnp.dot(first_part.T, second_part, precision=highest) + jnp.dot(second_part.T, first_part, precision=highest)
        return ((instant / pair_count).astype(jnp.bfloat16), (crossed / pair_count).astype(jnp.bfloat16))
    instant_cov, lagged_cov = lax.map(one_replicate, (resample, lag_time))
    return (instant_cov, lagged_cov)
```

```python
import jax
import jax.numpy as jnp
from jax import lax
from jax.sharding import PartitionSpec as P

F = 4096
ATOMS = 128
BLOCK_LEN = 32
DRAWS = 22


def gather_blocks(coordinates, resample, block_slot):
    groups = lax.axis_size("row") * lax.axis_size("col")
    if BLOCK_LEN % groups:
        groups = 1
    frames = BLOCK_LEN // groups
    member = lax.axis_index("row") * lax.axis_size("col") + lax.axis_index("col")
    if groups == 1:
        member = 0
    piece = lax.dynamic_slice_in_dim(coordinates, member * frames, frames, axis=1)
    every = lax.all_gather(piece, "rep", axis=0, tiled=True)
    slots = jnp.take(block_slot, resample[0], axis=0)
    picked = jnp.take(every, slots, axis=0)
    if groups == 1:
        return picked
    return lax.all_gather(picked, ("row", "col"), axis=1, tiled=True)


def tile_features(chosen, atom_pairs, first_feature, width, shift):
    first_atoms = lax.dynamic_slice_in_dim(atom_pairs[0], first_feature, width)
    second_atoms = lax.dynamic_slice_in_dim(atom_pairs[1], first_feature, width)
    atom_ids = jnp.arange(chosen.shape[-1], dtype=jnp.int32)[:, None]
    signed = (
        (atom_ids == first_atoms[None, :]).astype(jnp.float32)
        - (atom_ids == second_atoms[None, :]).astype(jnp.float32)
    ).astype(jnp.bfloat16)
    flat = chosen.reshape(-1, chosen.shape[-1])
    difference = jnp.dot(flat, signed, preferred_element_type=jnp.float32).reshape(
        DRAWS, BLOCK_LEN, 3, width
    )
    squared = (
        difference[:, :, 0] * difference[:, :, 0]
        + difference[:, :, 1] * difference[:, :, 1]
        + difference[:, :, 2] * difference[:, :, 2]
    )
    features = jnp.sqrt(squared).astype(jnp.bfloat16)
    doubled = jnp.concatenate([features, features], axis=1)
    shifted = lax.dynamic_slice_in_dim(doubled, shift, BLOCK_LEN, axis=1)
    valid_rows = (jnp.arange(BLOCK_LEN, dtype=jnp.int32) < BLOCK_LEN - shift)[None, :, None]
    pair_count = (2 * DRAWS * (BLOCK_LEN - shift)).astype(jnp.float32)
    earlier = jnp.where(valid_rows, features.astype(jnp.float32), 0.0)
    later = jnp.where(valid_rows, shifted.astype(jnp.float32), 0.0)
    feature_mean = (jnp.sum(earlier, axis=(0, 1)) + jnp.sum(later, axis=(0, 1))) / pair_count
    zero_lag = (
        jnp.where(valid_rows, earlier - feature_mean, 0.0).astype(jnp.bfloat16).reshape(-1, width)
    )
    lagged = (
        jnp.where(valid_rows, later - feature_mean, 0.0).astype(jnp.bfloat16).reshape(-1, width)
    )
    return (zero_lag, lagged, pair_count)


def shards(coordinates, resample, block_slot, lag_time, atom_pairs):
    chosen = gather_blocks(coordinates, resample, block_slot)
    width = F // lax.axis_size("row")
    shift = lag_time[0]
    zero_row, lag_row, pair_count = tile_features(
        chosen, atom_pairs, lax.axis_index("row") * width, width, shift
    )
    row_stack = jnp.concatenate([zero_row, lag_row], axis=0)
    zero_col, lag_col, unused_count = tile_features(
        chosen, atom_pairs, lax.axis_index("col") * width, width, shift
    )
    col_stack = jnp.concatenate([zero_col, lag_col], axis=0)
    half_rows = col_stack.shape[0] // 2
    mirrored = jnp.concatenate([col_stack[half_rows:], col_stack[:half_rows]], axis=0)
    instant = (
        jnp.einsum("na,nb->ab", row_stack, col_stack, preferred_element_type=jnp.float32)
        / pair_count
    )
    crossed = (
        jnp.einsum("na,nb->ab", row_stack, mirrored, preferred_element_type=jnp.float32)
        / pair_count
    )
    return (instant[None].astype(jnp.bfloat16), crossed[None].astype(jnp.bfloat16))


def solution(mesh):
    return jax.shard_map(
        shards,
        mesh=mesh,
        in_specs=(P("rep", None, None, None), P("rep", None), P(), P("rep"), P()),
        out_specs=(P("rep", "row", "col"), P("rep", "row", "col")),
        check_vma=False,
    )
```

```python
import functools

import jax
import jax.numpy as jnp
from jax import lax
from jax.experimental import pallas as pl
from jax.experimental.pallas import tpu as pltpu
from jax.sharding import PartitionSpec as P

F = 4096
ATOMS = 128
BLOCK_LEN = 32
DRAWS = 22
TILE = 256


def gather_blocks(coordinates, resample, block_slot):
    groups = lax.axis_size("row") * lax.axis_size("col")
    if BLOCK_LEN % groups:
        groups = 1
    frames = BLOCK_LEN // groups
    member = lax.axis_index("row") * lax.axis_size("col") + lax.axis_index("col")
    if groups == 1:
        member = 0
    piece = lax.dynamic_slice_in_dim(coordinates, member * frames, frames, axis=1)
    reps = lax.axis_size("rep")
    spread = jnp.broadcast_to(piece[None], (reps,) + piece.shape)
    every = lax.all_to_all(spread, "rep", 0, 0, tiled=True)
    every = every.reshape((-1,) + piece.shape[1:])
    slots = jnp.take(block_slot, resample[0], axis=0)
    picked = jnp.take(every, slots, axis=0)
    if groups == 1:
        return picked
    spread = jnp.broadcast_to(picked[None], (groups,) + picked.shape)
    parts = lax.all_to_all(spread, ("row", "col"), 0, 0, tiled=True)
    return jnp.swapaxes(parts, 0, 1).reshape(DRAWS, BLOCK_LEN, 3, ATOMS)


def centered_kernel(lag_ref, x_ref, xs_ref, s_ref, out_ref):
    lag = lag_ref[0]
    signed = s_ref[...]

    def distances(ref):
        total = None
        for c in range(3):
            d = jnp.dot(ref[c], signed, preferred_element_type=jnp.float32)
            total = d * d if total is None else total + d * d
        return jnp.sqrt(total).astype(jnp.bfloat16).astype(jnp.float32)

    earlier = distances(x_ref)
    later = distances(xs_ref)
    rows = lax.broadcasted_iota(jnp.int32, earlier.shape, 0)
    valid = (rows % BLOCK_LEN) < (BLOCK_LEN - lag)
    earlier = jnp.where(valid, earlier, 0.0)
    later = jnp.where(valid, later, 0.0)
    count = (2 * DRAWS * (BLOCK_LEN - lag)).astype(jnp.float32)
    mean = (
        jnp.sum(earlier, axis=0, keepdims=True) + jnp.sum(later, axis=0, keepdims=True)
    ) / count
    out_ref[0] = jnp.where(valid, earlier - mean, 0.0).astype(jnp.bfloat16)
    out_ref[1] = jnp.where(valid, later - mean, 0.0).astype(jnp.bfloat16)


def centered_pairs(lag, frames, shifted, signed):
    n = frames.shape[1]
    width = signed.shape[1]
    return pl.pallas_call(
        centered_kernel,
        grid=(width // TILE,),
        in_specs=[
            pl.BlockSpec(memory_space=pltpu.SMEM),
            pl.BlockSpec((3, n, ATOMS), lambda j: (0, 0, 0)),
            pl.BlockSpec((3, n, ATOMS), lambda j: (0, 0, 0)),
            pl.BlockSpec((ATOMS, TILE), lambda j: (0, j)),
        ],
        out_specs=pl.BlockSpec((2, n, TILE), lambda j: (0, 0, j)),
        out_shape=jax.ShapeDtypeStruct((2, n, width), jnp.bfloat16),
        cost_estimate=pl.CostEstimate(
            flops=2 * 2 * 3 * n * ATOMS * width,
            transcendentals=2 * n * width,
            bytes_accessed=2 * n * width * 2 + 2 * 3 * n * ATOMS * 2 + ATOMS * width * 2,
        ),
    )(lag, frames, shifted, signed)


def signed_pairs(atom_pairs, first_feature, width):
    first_atoms = lax.dynamic_slice_in_dim(atom_pairs[0], first_feature, width)
    second_atoms = lax.dynamic_slice_in_dim(atom_pairs[1], first_feature, width)
    atom_ids = jnp.arange(ATOMS, dtype=jnp.int32)[:, None]
    return (
        (atom_ids == first_atoms[None, :]).astype(jnp.float32)
        - (atom_ids == second_atoms[None, :]).astype(jnp.float32)
    ).astype(jnp.bfloat16)


def shards(coordinates, resample, block_slot, lag_time, atom_pairs):
    chosen = gather_blocks(coordinates, resample, block_slot)
    width = F // lax.axis_size("row")
    shift = lag_time[0]
    doubled = jnp.concatenate([chosen, chosen], axis=1)
    moved = lax.dynamic_slice_in_dim(doubled, shift, BLOCK_LEN, axis=1)
    frames = jnp.transpose(chosen, (2, 0, 1, 3)).reshape(3, DRAWS * BLOCK_LEN, ATOMS)
    shifted = jnp.transpose(moved, (2, 0, 1, 3)).reshape(3, DRAWS * BLOCK_LEN, ATOMS)
    row_signed = signed_pairs(atom_pairs, lax.axis_index("row") * width, width)
    col_signed = signed_pairs(atom_pairs, lax.axis_index("col") * width, width)
    row_stack = centered_pairs(lag_time, frames, shifted, row_signed)
    col_stack = centered_pairs(lag_time, frames, shifted, col_signed)
    pair_count = (2 * DRAWS * (BLOCK_LEN - shift)).astype(jnp.float32)
    rows = row_stack.reshape(-1, width)
    instant = (
        jnp.einsum("na,nb->ab", rows, col_stack.reshape(-1, width), preferred_element_type=jnp.float32)
        / pair_count
    )
    crossed = (
        jnp.einsum("na,nb->ab", rows, col_stack[::-1].reshape(-1, width), preferred_element_type=jnp.float32)
        / pair_count
    )
    return (instant[None].astype(jnp.bfloat16), crossed[None].astype(jnp.bfloat16))


def solution(mesh):
    return jax.shard_map(
        shards,
        mesh=mesh,
        in_specs=(P("rep", None, None, None), P("rep", None), P(), P("rep"), P()),
        out_specs=(P("rep", "row", "col"), P("rep", "row", "col")),
        check_vma=False,
    )
```

```python
import functools

import jax
import jax.numpy as jnp
from jax import lax
from jax.experimental import pallas as pl
from jax.experimental.pallas import tpu as pltpu
from jax.sharding import PartitionSpec as P

F = 4096
ATOMS = 128
BLOCK_LEN = 32
DRAWS = 22
TILE = 512


def gather_blocks(coordinates, resample, block_slot):
    groups = lax.axis_size("row") * lax.axis_size("col")
    if BLOCK_LEN % groups:
        groups = 1
    frames = BLOCK_LEN // groups
    member = lax.axis_index("row") * lax.axis_size("col") + lax.axis_index("col")
    if groups == 1:
        member = 0
    piece = lax.dynamic_slice_in_dim(coordinates, member * frames, frames, axis=1)
    reps = lax.axis_size("rep")
    spread = jnp.broadcast_to(piece[None], (reps,) + piece.shape)
    every = lax.all_to_all(spread, "rep", 0, 0, tiled=True)
    every = every.reshape((-1,) + piece.shape[1:])
    slots = jnp.take(block_slot, resample[0], axis=0)
    picked = jnp.take(every, slots, axis=0)
    if groups == 1:
        return picked
    spread = jnp.broadcast_to(picked[None], (groups,) + picked.shape)
    parts = lax.all_to_all(spread, ("row", "col"), 0, 0, tiled=True)
    return jnp.swapaxes(parts, 0, 1).reshape(DRAWS, BLOCK_LEN, 3, ATOMS)


def centered_kernel(planes, lag_ref, x_ref, s_ref, out_ref):
    lag = lag_ref[0]
    signed = s_ref[...]
    total = None
    for c in range(3):
        d = jnp.dot(x_ref[c], signed, preferred_element_type=jnp.float32)
        total = d * d if total is None else total + d * d
    earlier = jnp.sqrt(total).astype(jnp.bfloat16).astype(jnp.float32)
    n = earlier.shape[0]
    later = pltpu.roll(earlier, n - lag, 0)
    rows = lax.broadcasted_iota(jnp.int32, earlier.shape, 0)
    valid = (rows % BLOCK_LEN) < (BLOCK_LEN - lag)
    earlier = jnp.where(valid, earlier, 0.0)
    later = jnp.where(valid, later, 0.0)
    count = (2 * DRAWS * (BLOCK_LEN - lag)).astype(jnp.float32)
    mean = (
        jnp.sum(earlier, axis=0, keepdims=True) + jnp.sum(later, axis=0, keepdims=True)
    ) / count
    zero_lag = jnp.where(valid, earlier - mean, 0.0).astype(jnp.bfloat16)
    out_ref[0] = zero_lag
    out_ref[1] = jnp.where(valid, later - mean, 0.0).astype(jnp.bfloat16)
    if planes == 3:
        out_ref[2] = zero_lag


def centered_pairs(lag, frames, signed, planes):
    n = frames.shape[1]
    width = signed.shape[1]
    return pl.pallas_call(
        functools.partial(centered_kernel, planes),
        grid=(width // TILE,),
        in_specs=[
            pl.BlockSpec(memory_space=pltpu.SMEM),
            pl.BlockSpec((3, n, ATOMS), lambda j: (0, 0, 0)),
            pl.BlockSpec((ATOMS, TILE), lambda j: (0, j)),
        ],
        out_specs=pl.BlockSpec((planes, n, TILE), lambda j: (0, 0, j)),
        out_shape=jax.ShapeDtypeStruct((planes, n, width), jnp.bfloat16),
        cost_estimate=pl.CostEstimate(
            flops=2 * 3 * n * ATOMS * width,
            transcendentals=n * width,
            bytes_accessed=planes * n * width * 2 + 3 * n * ATOMS * 2 + ATOMS * width * 2,
        ),
    )(lag, frames, signed)


def signed_pairs(atom_pairs, first_feature, width):
    first_atoms = lax.dynamic_slice_in_dim(atom_pairs[0], first_feature, width)
    second_atoms = lax.dynamic_slice_in_dim(atom_pairs[1], first_feature, width)
    atom_ids = jnp.arange(ATOMS, dtype=jnp.int32)[:, None]
    return (
        (atom_ids == first_atoms[None, :]).astype(jnp.float32)
        - (atom_ids == second_atoms[None, :]).astype(jnp.float32)
    ).astype(jnp.bfloat16)


def shards(coordinates, resample, block_slot, lag_time, atom_pairs):
    chosen = gather_blocks(coordinates, resample, block_slot)
    width = F // lax.axis_size("row")
    shift = lag_time[0]
    frames = jnp.transpose(chosen, (2, 0, 1, 3)).reshape(3, DRAWS * BLOCK_LEN, ATOMS)
    row_signed = signed_pairs(atom_pairs, lax.axis_index("row") * width, width)
    col_signed = signed_pairs(atom_pairs, lax.axis_index("col") * width, width)
    row_stack = centered_pairs(lag_time, frames, row_signed, 2).reshape(-1, width)
    col_stack = centered_pairs(lag_time, frames, col_signed, 3)
    pair_count = (2 * DRAWS * (BLOCK_LEN - shift)).astype(jnp.float32)
    instant = (
        jnp.einsum("na,nb->ab", row_stack, col_stack[:2].reshape(-1, width), preferred_element_type=jnp.float32)
        / pair_count
    )
    crossed = (
        jnp.einsum("na,nb->ab", row_stack, col_stack[1:].reshape(-1, width), preferred_element_type=jnp.float32)
        / pair_count
    )
    return (instant[None].astype(jnp.bfloat16), crossed[None].astype(jnp.bfloat16))


def solution(mesh):
    return jax.shard_map(
        shards,
        mesh=mesh,
        in_specs=(P("rep", None, None, None), P("rep", None), P(), P("rep"), P()),
        out_specs=(P("rep", "row", "col"), P("rep", "row", "col")),
        check_vma=False,
    )
```

```python
import functools

import jax
import jax.numpy as jnp
from jax import lax
from jax.experimental import pallas as pl
from jax.experimental.pallas import tpu as pltpu
from jax.sharding import PartitionSpec as P

F = 4096
ATOMS = 128
BLOCK_LEN = 32
DRAWS = 22
TILE = 512


def gather_blocks(coordinates, resample, block_slot):
    groups = lax.axis_size("row") * lax.axis_size("col")
    if BLOCK_LEN % groups:
        groups = 1
    frames = BLOCK_LEN // groups
    member = lax.axis_index("row") * lax.axis_size("col") + lax.axis_index("col")
    if groups == 1:
        member = 0
    piece = lax.dynamic_slice_in_dim(coordinates, member * frames, frames, axis=1)
    reps = lax.axis_size("rep")
    spread = jnp.broadcast_to(piece[None], (reps,) + piece.shape)
    every = lax.all_to_all(spread, "rep", 0, 0, tiled=True)
    every = every.reshape((-1,) + piece.shape[1:])
    slots = jnp.take(block_slot, resample[0], axis=0)
    picked = jnp.take(every, slots, axis=0)
    if groups == 1:
        return picked
    spread = jnp.broadcast_to(picked[None], (groups,) + picked.shape)
    parts = lax.all_to_all(spread, ("row", "col"), 0, 0, tiled=True)
    return jnp.swapaxes(parts, 0, 1).reshape(DRAWS, BLOCK_LEN, 3, ATOMS)


def centered_kernel(planes, lag_ref, x_ref, s_ref, out_ref, diff_ref, dist_ref):
    lag = lag_ref[0]
    signed = s_ref[...]
    for c in range(3):
        diff_ref[c] = jnp.dot(x_ref[c], signed, preferred_element_type=jnp.float32)
    width = signed.shape[1]
    frame = lax.broadcasted_iota(jnp.int32, (BLOCK_LEN, width), 0)
    first = frame < BLOCK_LEN - lag
    second = frame >= lag
    dist_ref[pl.ds(DRAWS * BLOCK_LEN, BLOCK_LEN), :] = jnp.zeros((BLOCK_LEN, width), jnp.float32)

    def distances(d, sums):
        rows = pl.ds(pl.multiple_of(d * BLOCK_LEN, BLOCK_LEN), BLOCK_LEN)
        total = None
        for c in range(3):
            part = diff_ref[c, rows, :]
            total = part * part if total is None else total + part * part
        dist = jnp.sqrt(total).astype(jnp.bfloat16).astype(jnp.float32)
        dist_ref[rows, :] = dist
        picked = jnp.where(first, dist, 0.0) + jnp.where(second, dist, 0.0)
        return sums + picked.reshape(BLOCK_LEN // 8, 8, width).sum(axis=0)

    sums = lax.fori_loop(0, DRAWS, distances, jnp.zeros((8, width), jnp.float32))
    count = (2 * DRAWS * (BLOCK_LEN - lag)).astype(jnp.float32)
    mean = jnp.sum(sums, axis=0, keepdims=True) / count

    def center(d, carry):
        start = pl.multiple_of(d * BLOCK_LEN, BLOCK_LEN)
        rows = pl.ds(start, BLOCK_LEN)
        earlier = dist_ref[rows, :]
        window = dist_ref[pl.ds(start, 2 * BLOCK_LEN), :]
        later = pltpu.roll(window, 2 * BLOCK_LEN - lag, 0)[:BLOCK_LEN]
        zero_lag = jnp.where(first, earlier - mean, 0.0).astype(jnp.bfloat16)
        out_ref[0, rows, :] = zero_lag
        out_ref[1, rows, :] = jnp.where(first, later - mean, 0.0).astype(jnp.bfloat16)
        if planes == 3:
            out_ref[2, rows, :] = zero_lag
        return carry

    lax.fori_loop(0, DRAWS, center, 0)


def centered_pairs(lag, frames, signed, planes):
    n = frames.shape[1]
    width = signed.shape[1]
    return pl.pallas_call(
        functools.partial(centered_kernel, planes),
        grid=(width // TILE,),
        in_specs=[
            pl.BlockSpec(memory_space=pltpu.SMEM),
            pl.BlockSpec((3, n, ATOMS), lambda j: (0, 0, 0)),
            pl.BlockSpec((ATOMS, TILE), lambda j: (0, j)),
        ],
        out_specs=pl.BlockSpec((planes, n, TILE), lambda j: (0, 0, j)),
        out_shape=jax.ShapeDtypeStruct((planes, n, width), jnp.bfloat16),
        scratch_shapes=[
            pltpu.VMEM((3, n, TILE), jnp.float32),
            pltpu.VMEM((n + BLOCK_LEN, TILE), jnp.float32),
        ],
        cost_estimate=pl.CostEstimate(
            flops=2 * 3 * n * ATOMS * width,
            transcendentals=n * width,
            bytes_accessed=planes * n * width * 2 + 3 * n * ATOMS * 2 + ATOMS * width * 2,
        ),
    )(lag, frames, signed)


def signed_pairs(atom_pairs, first_feature, width):
    first_atoms = lax.dynamic_slice_in_dim(atom_pairs[0], first_feature, width)
    second_atoms = lax.dynamic_slice_in_dim(atom_pairs[1], first_feature, width)
    atom_ids = jnp.arange(ATOMS, dtype=jnp.int32)[:, None]
    return (
        (atom_ids == first_atoms[None, :]).astype(jnp.float32)
        - (atom_ids == second_atoms[None, :]).astype(jnp.float32)
    ).astype(jnp.bfloat16)


def shards(coordinates, resample, block_slot, lag_time, atom_pairs):
    chosen = gather_blocks(coordinates, resample, block_slot)
    width = F // lax.axis_size("row")
    shift = lag_time[0]
    frames = jnp.transpose(chosen, (2, 0, 1, 3)).reshape(3, DRAWS * BLOCK_LEN, ATOMS)
    row_signed = signed_pairs(atom_pairs, lax.axis_index("row") * width, width)
    col_signed = signed_pairs(atom_pairs, lax.axis_index("col") * width, width)
    row_stack = centered_pairs(lag_time, frames, row_signed, 2).reshape(-1, width)
    col_stack = centered_pairs(lag_time, frames, col_signed, 3)
    pair_count = (2 * DRAWS * (BLOCK_LEN - shift)).astype(jnp.float32)
    instant = (
        jnp.einsum("na,nb->ab", row_stack, col_stack[:2].reshape(-1, width), preferred_element_type=jnp.float32)
        / pair_count
    )
    crossed = (
        jnp.einsum("na,nb->ab", row_stack, col_stack[1:].reshape(-1, width), preferred_element_type=jnp.float32)
        / pair_count
    )
    return (instant[None].astype(jnp.bfloat16), crossed[None].astype(jnp.bfloat16))


def solution(mesh):
    return jax.shard_map(
        shards,
        mesh=mesh,
        in_specs=(P("rep", None, None, None), P("rep", None), P(), P("rep"), P()),
        out_specs=(P("rep", "row", "col"), P("rep", "row", "col")),
        check_vma=False,
    )
```

```python
import functools

import jax
import jax.numpy as jnp
from jax import lax
from jax.experimental import pallas as pl
from jax.experimental.pallas import tpu as pltpu
from jax.sharding import PartitionSpec as P

F = 4096
ATOMS = 128
BLOCK_LEN = 32
DRAWS = 22
CHUNK = 128
OUT_BLOCK = 256


def gather_blocks(coordinates, resample, block_slot):
    groups = lax.axis_size("row") * lax.axis_size("col")
    if BLOCK_LEN % groups:
        groups = 1
    frames = BLOCK_LEN // groups
    member = lax.axis_index("row") * lax.axis_size("col") + lax.axis_index("col")
    if groups == 1:
        member = 0
    piece = lax.dynamic_slice_in_dim(coordinates, member * frames, frames, axis=1)
    reps = lax.axis_size("rep")
    spread = jnp.broadcast_to(piece[None], (reps,) + piece.shape)
    every = lax.all_to_all(spread, "rep", 0, 0, tiled=True)
    every = every.reshape((-1,) + piece.shape[1:])
    slots = jnp.take(block_slot, resample[0], axis=0)
    picked = jnp.take(every, slots, axis=0)
    if groups == 1:
        return picked
    spread = jnp.broadcast_to(picked[None], (groups,) + picked.shape)
    parts = lax.all_to_all(spread, ("row", "col"), 0, 0, tiled=True)
    return jnp.swapaxes(parts, 0, 1).reshape(DRAWS, BLOCK_LEN, 3, ATOMS)


def covariance_kernel(lag_ref, x_ref, sr_ref, sc_ref, inst_ref, cross_ref, stack_ref):
    lag = lag_ref[0]
    lanes = x_ref.shape[2]
    count = (2 * DRAWS * (BLOCK_LEN - lag)).astype(jnp.float32)

    @pl.when(pl.program_id(0) == 0)
    def _():
        pair = lax.broadcasted_iota(jnp.int32, (1, lanes), 1)
        first = ((pair % BLOCK_LEN) < (BLOCK_LEN - lag)) & (pair < DRAWS * BLOCK_LEN)

        per_tile = sr_ref.shape[0] // CHUNK

        def centered(i, carry):
            tile = i // per_tile
            start = pl.multiple_of((i % per_tile) * CHUNK, CHUNK)
            rows = pl.ds(start, CHUNK)
            signed = jnp.where(tile == 0, sr_ref[rows, :], sc_ref[rows, :])
            total = None
            for c in range(3):
                d = jnp.dot(signed, x_ref[c], preferred_element_type=jnp.float32)
                total = d * d if total is None else total + d * d
            dist = jnp.sqrt(total).astype(jnp.bfloat16).astype(jnp.float32)
            later = pltpu.roll(dist, lanes - lag, 1)
            earlier = jnp.where(first, dist, 0.0)
            later = jnp.where(first, later, 0.0)
            mean = (
                jnp.sum(earlier, axis=1, keepdims=True) + jnp.sum(later, axis=1, keepdims=True)
            ) / count
            stack_ref[2 * tile, rows, :] = jnp.where(first, earlier - mean, 0.0).astype(jnp.bfloat16)
            stack_ref[2 * tile + 1, rows, :] = jnp.where(first, later - mean, 0.0).astype(jnp.bfloat16)
            return carry

        lax.fori_loop(0, 2 * per_tile, centered, 0)

    block = inst_ref.shape[0]
    rows = pl.ds(pl.multiple_of(pl.program_id(0) * block, block), block)
    nt = (((1,), (1,)), ((), ()))
    zero_row = stack_ref[0, rows, :]
    lag_row = stack_ref[1, rows, :]
    zero_col = stack_ref[2]
    lag_col = stack_ref[3]
    instant = lax.dot_general(zero_row, zero_col, nt, preferred_element_type=jnp.float32)
    instant = instant + lax.dot_general(lag_row, lag_col, nt, preferred_element_type=jnp.float32)
    inst_ref[...] = (instant / count).astype(inst_ref.dtype)
    crossed = lax.dot_general(zero_row, lag_col, nt, preferred_element_type=jnp.float32)
    crossed = crossed + lax.dot_general(lag_row, zero_col, nt, preferred_element_type=jnp.float32)
    cross_ref[...] = (crossed / count).astype(cross_ref.dtype)


def covariances(lag, frames, row_signed, col_signed):
    lanes = frames.shape[2]
    width = row_signed.shape[0]
    out = jax.ShapeDtypeStruct((width, width), jnp.bfloat16)
    return pl.pallas_call(
        covariance_kernel,
        grid=(width // OUT_BLOCK,),
        in_specs=[
            pl.BlockSpec(memory_space=pltpu.SMEM),
            pl.BlockSpec((3, ATOMS, lanes), lambda j: (0, 0, 0)),
            pl.BlockSpec((width, ATOMS), lambda j: (0, 0)),
            pl.BlockSpec((width, ATOMS), lambda j: (0, 0)),
        ],
        out_specs=[
            pl.BlockSpec((OUT_BLOCK, width), lambda j: (j, 0)),
            pl.BlockSpec((OUT_BLOCK, width), lambda j: (j, 0)),
        ],
        out_shape=[out, out],
        scratch_shapes=[pltpu.VMEM((4, width, lanes), jnp.bfloat16)],
        compiler_params=pltpu.CompilerParams(dimension_semantics=("arbitrary",)),
        cost_estimate=pl.CostEstimate(
            flops=2 * 2 * 3 * width * ATOMS * lanes + 4 * 2 * width * width * lanes,
            transcendentals=2 * width * lanes,
            bytes_accessed=2 * width * width * 2 + 3 * ATOMS * lanes * 2 + 2 * width * ATOMS * 2,
        ),
    )(lag, frames, row_signed, col_signed)


def signed_pairs(atom_pairs, first_feature, width):
    first_atoms = lax.dynamic_slice_in_dim(atom_pairs[0], first_feature, width)
    second_atoms = lax.dynamic_slice_in_dim(atom_pairs[1], first_feature, width)
    atom_ids = jnp.arange(ATOMS, dtype=jnp.int32)[None, :]
    return (
        (first_atoms[:, None] == atom_ids).astype(jnp.float32)
        - (second_atoms[:, None] == atom_ids).astype(jnp.float32)
    ).astype(jnp.bfloat16)


def shards(coordinates, resample, block_slot, lag_time, atom_pairs):
    chosen = gather_blocks(coordinates, resample, block_slot)
    width = F // lax.axis_size("row")
    pairs = DRAWS * BLOCK_LEN
    lanes = -(-pairs // 128) * 128
    frames = jnp.transpose(chosen, (2, 3, 0, 1)).reshape(3, ATOMS, pairs)
    frames = jnp.pad(frames, ((0, 0), (0, 0), (0, lanes - pairs)))
    row_signed = signed_pairs(atom_pairs, lax.axis_index("row") * width, width)
    col_signed = signed_pairs(atom_pairs, lax.axis_index("col") * width, width)
    instant, crossed = covariances(lag_time, frames, row_signed, col_signed)
    return (instant[None], crossed[None])


def solution(mesh):
    return jax.shard_map(
        shards,
        mesh=mesh,
        in_specs=(P("rep", None, None, None), P("rep", None), P(), P("rep"), P()),
        out_specs=(P("rep", "row", "col"), P("rep", "row", "col")),
        check_vma=False,
    )
```

```python
import functools

import jax
import jax.numpy as jnp
from jax import lax
from jax.experimental import pallas as pl
from jax.experimental.pallas import tpu as pltpu
from jax.sharding import PartitionSpec as P

F = 4096
ATOMS = 128
BLOCK_LEN = 32
DRAWS = 22
CHUNK = 128
OUT_BLOCK = 256


def gather_blocks(coordinates, resample, block_slot):
    groups = lax.axis_size("row") * lax.axis_size("col")
    if BLOCK_LEN % groups:
        groups = 1
    frames = BLOCK_LEN // groups
    member = lax.axis_index("row") * lax.axis_size("col") + lax.axis_index("col")
    if groups == 1:
        member = 0
    piece = lax.dynamic_slice_in_dim(coordinates, member * frames, frames, axis=1)
    reps = lax.axis_size("rep")
    spread = jnp.broadcast_to(piece[None], (reps,) + piece.shape)
    every = lax.all_to_all(spread, "rep", 0, 0, tiled=True)
    every = every.reshape((-1,) + piece.shape[1:])
    slots = jnp.take(block_slot, resample[0], axis=0)
    picked = jnp.take(every, slots, axis=0)
    if groups == 1:
        return picked
    spread = jnp.broadcast_to(picked[None], (groups,) + picked.shape)
    parts = lax.all_to_all(spread, ("row", "col"), 0, 0, tiled=True)
    return jnp.swapaxes(parts, 0, 1).reshape(DRAWS, BLOCK_LEN, 3, ATOMS)


def covariance_kernel(lag_ref, x_ref, mask_ref, sr_ref, sc_ref, inst_ref, cross_ref, row_ref, col_ref, swap_ref):
    lag = lag_ref[0]
    lanes = x_ref.shape[2]
    count = (2 * DRAWS * (BLOCK_LEN - lag)).astype(jnp.float32)

    @pl.when(pl.program_id(0) == 0)
    def _():
        pair = lax.broadcasted_iota(jnp.int32, (1, lanes), 1)
        first = ((pair % BLOCK_LEN) < (BLOCK_LEN - lag)) & (pair < DRAWS * BLOCK_LEN)
        per_tile = sr_ref.shape[0] // CHUNK

        def distances(signed):
            total = None
            for c in range(3):
                d = jnp.dot(signed, x_ref[c], preferred_element_type=jnp.float32)
                total = d * d if total is None else total + d * d
            dist = jnp.sqrt(total).astype(jnp.bfloat16)
            sums = jnp.dot(dist, mask_ref[...], preferred_element_type=jnp.float32)
            mean = (sums[:, 0:1] + sums[:, 1:2]) / count
            dist = dist.astype(jnp.float32)
            return dist, pltpu.roll(dist, lanes - lag, 1), mean

        def row_tile(i, carry):
            rows = pl.ds(pl.multiple_of(i * CHUNK, CHUNK), CHUNK)
            earlier, later, mean = distances(sr_ref[rows, :])
            row_ref[rows, :lanes] = jnp.where(first, earlier - mean, 0.0).astype(jnp.bfloat16)
            row_ref[rows, lanes:] = jnp.where(first, later - mean, 0.0).astype(jnp.bfloat16)
            return carry

        def col_tile(i, carry):
            rows = pl.ds(pl.multiple_of(i * CHUNK, CHUNK), CHUNK)
            earlier, later, mean = distances(sc_ref[rows, :])
            zero_lag = (earlier - mean).astype(jnp.bfloat16)
            lagged = (later - mean).astype(jnp.bfloat16)
            col_ref[rows, :lanes] = zero_lag
            col_ref[rows, lanes:] = lagged
            swap_ref[rows, :lanes] = lagged
            swap_ref[rows, lanes:] = zero_lag
            return carry

        lax.fori_loop(0, per_tile, row_tile, 0)
        lax.fori_loop(0, per_tile, col_tile, 0)

    block = inst_ref.shape[0]
    rows = pl.ds(pl.multiple_of(pl.program_id(0) * block, block), block)
    nt = (((1,), (1,)), ((), ()))
    stacked = row_ref[rows, :]
    instant = lax.dot_general(stacked, col_ref[...], nt, preferred_element_type=jnp.float32)
    inst_ref[...] = (instant / count).astype(inst_ref.dtype)
    crossed = lax.dot_general(stacked, swap_ref[...], nt, preferred_element_type=jnp.float32)
    cross_ref[...] = (crossed / count).astype(cross_ref.dtype)


def covariances(lag, frames, mask, row_signed, col_signed):
    lanes = frames.shape[2]
    width = row_signed.shape[0]
    out = jax.ShapeDtypeStruct((width, width), jnp.bfloat16)
    return pl.pallas_call(
        covariance_kernel,
        grid=(width // OUT_BLOCK,),
        in_specs=[
            pl.BlockSpec(memory_space=pltpu.SMEM),
            pl.BlockSpec((3, ATOMS, lanes), lambda j: (0, 0, 0)),
            pl.BlockSpec((lanes, 128), lambda j: (0, 0)),
            pl.BlockSpec((width, ATOMS), lambda j: (0, 0)),
            pl.BlockSpec((width, ATOMS), lambda j: (0, 0)),
        ],
        out_specs=[
            pl.BlockSpec((OUT_BLOCK, width), lambda j: (j, 0)),
            pl.BlockSpec((OUT_BLOCK, width), lambda j: (j, 0)),
        ],
        out_shape=[out, out],
        scratch_shapes=[pltpu.VMEM((width, 2 * lanes), jnp.bfloat16)] * 3,
        compiler_params=pltpu.CompilerParams(dimension_semantics=("arbitrary",)),
        cost_estimate=pl.CostEstimate(
            flops=2 * 2 * 3 * width * ATOMS * lanes + 4 * 2 * width * width * lanes,
            transcendentals=2 * width * lanes,
            bytes_accessed=2 * width * width * 2 + 3 * ATOMS * lanes * 2 + 2 * width * ATOMS * 2,
        ),
    )(lag, frames, mask, row_signed, col_signed)


def pair_masks(shift, lanes):
    pair = jnp.arange(lanes, dtype=jnp.int32)
    frame = pair % BLOCK_LEN
    inside = pair < DRAWS * BLOCK_LEN
    first = inside & (frame < BLOCK_LEN - shift)
    second = inside & (frame >= shift)
    column = jnp.arange(128, dtype=jnp.int32)[None, :]
    mask = jnp.where(column == 0, first[:, None], False) | jnp.where(column == 1, second[:, None], False)
    return mask.astype(jnp.bfloat16)


def signed_pairs(atom_pairs, first_feature, width):
    first_atoms = lax.dynamic_slice_in_dim(atom_pairs[0], first_feature, width)
    second_atoms = lax.dynamic_slice_in_dim(atom_pairs[1], first_feature, width)
    atom_ids = jnp.arange(ATOMS, dtype=jnp.int32)[None, :]
    return (
        (first_atoms[:, None] == atom_ids).astype(jnp.float32)
        - (second_atoms[:, None] == atom_ids).astype(jnp.float32)
    ).astype(jnp.bfloat16)


def shards(coordinates, resample, block_slot, lag_time, atom_pairs):
    chosen = gather_blocks(coordinates, resample, block_slot)
    width = F // lax.axis_size("row")
    pairs = DRAWS * BLOCK_LEN
    lanes = -(-pairs // 128) * 128
    frames = jnp.transpose(chosen, (2, 3, 0, 1)).reshape(3, ATOMS, pairs)
    frames = jnp.pad(frames, ((0, 0), (0, 0), (0, lanes - pairs)))
    row_signed = signed_pairs(atom_pairs, lax.axis_index("row") * width, width)
    col_signed = signed_pairs(atom_pairs, lax.axis_index("col") * width, width)
    mask = pair_masks(lag_time[0], lanes)
    instant, crossed = covariances(lag_time, frames, mask, row_signed, col_signed)
    return (instant[None], crossed[None])


def solution(mesh):
    return jax.shard_map(
        shards,
        mesh=mesh,
        in_specs=(P("rep", None, None, None), P("rep", None), P(), P("rep"), P()),
        out_specs=(P("rep", "row", "col"), P("rep", "row", "col")),
        check_vma=False,
    )
```

```python
import functools

import jax
import jax.numpy as jnp
from jax import lax
from jax.experimental import pallas as pl
from jax.experimental.pallas import tpu as pltpu
from jax.sharding import PartitionSpec as P

F = 4096
ATOMS = 128
BLOCK_LEN = 32
DRAWS = 22
OUT_BLOCK = 1024


def gather_blocks(coordinates, resample, block_slot):
    groups = lax.axis_size("row") * lax.axis_size("col")
    if BLOCK_LEN % groups:
        groups = 1
    frames = BLOCK_LEN // groups
    member = lax.axis_index("row") * lax.axis_size("col") + lax.axis_index("col")
    if groups == 1:
        member = 0
    piece = lax.dynamic_slice_in_dim(coordinates, member * frames, frames, axis=1)
    reps = lax.axis_size("rep")
    spread = jnp.broadcast_to(piece[None], (reps,) + piece.shape)
    every = lax.all_to_all(spread, "rep", 0, 0, tiled=True)
    every = every.reshape((-1,) + piece.shape[1:])
    slots = jnp.take(block_slot, resample[0], axis=0)
    picked = jnp.take(every, slots, axis=0)
    if groups == 1:
        return picked
    spread = jnp.broadcast_to(picked[None], (groups,) + picked.shape)
    parts = lax.all_to_all(spread, ("row", "col"), 0, 0, tiled=True)
    return jnp.swapaxes(parts, 0, 1).reshape(DRAWS, BLOCK_LEN, 3, ATOMS)


def covariance_kernel(lag_ref, x_ref, sr_ref, sc_ref, inst_ref, cross_ref, stack_ref):
    lag = lag_ref[0]
    lanes = x_ref.shape[2]
    count = (2 * DRAWS * (BLOCK_LEN - lag)).astype(jnp.float32)

    @pl.when(pl.program_id(0) == 0)
    def _():
        pair = lax.broadcasted_iota(jnp.int32, (1, lanes), 1)
        first = ((pair % BLOCK_LEN) < (BLOCK_LEN - lag)) & (pair < DRAWS * BLOCK_LEN)

        for tile, signed_ref in enumerate((sr_ref, sc_ref)):
            signed = signed_ref[...]
            total = None
            for c in range(3):
                d = jnp.dot(signed, x_ref[c], preferred_element_type=jnp.float32)
                total = d * d if total is None else total + d * d
            dist = jnp.sqrt(total).astype(jnp.bfloat16).astype(jnp.float32)
            later = pltpu.roll(dist, lanes - lag, 1)
            earlier = jnp.where(first, dist, 0.0)
            later = jnp.where(first, later, 0.0)
            mean = (
                jnp.sum(earlier, axis=1, keepdims=True) + jnp.sum(later, axis=1, keepdims=True)
            ) / count
            stack_ref[2 * tile] = jnp.where(first, earlier - mean, 0.0).astype(jnp.bfloat16)
            stack_ref[2 * tile + 1] = jnp.where(first, later - mean, 0.0).astype(jnp.bfloat16)

    block = inst_ref.shape[0]
    rows = pl.ds(pl.multiple_of(pl.program_id(0) * block, block), block)
    nt = (((1,), (1,)), ((), ()))
    zero_row = stack_ref[0, rows, :]
    lag_row = stack_ref[1, rows, :]
    zero_col = stack_ref[2]
    lag_col = stack_ref[3]
    instant = lax.dot_general(zero_row, zero_col, nt, preferred_element_type=jnp.float32)
    instant = instant + lax.dot_general(lag_row, lag_col, nt, preferred_element_type=jnp.float32)
    inst_ref[...] = (instant / count).astype(inst_ref.dtype)
    crossed = lax.dot_general(zero_row, lag_col, nt, preferred_element_type=jnp.float32)
    crossed = crossed + lax.dot_general(lag_row, zero_col, nt, preferred_element_type=jnp.float32)
    cross_ref[...] = (crossed / count).astype(cross_ref.dtype)


def covariances(lag, frames, row_signed, col_signed):
    lanes = frames.shape[2]
    width = row_signed.shape[0]
    out = jax.ShapeDtypeStruct((width, width), jnp.bfloat16)
    return pl.pallas_call(
        covariance_kernel,
        grid=(pl.cdiv(width, OUT_BLOCK),),
        in_specs=[
            pl.BlockSpec(memory_space=pltpu.SMEM),
            pl.BlockSpec((3, ATOMS, lanes), lambda j: (0, 0, 0)),
            pl.BlockSpec((width, ATOMS), lambda j: (0, 0)),
            pl.BlockSpec((width, ATOMS), lambda j: (0, 0)),
        ],
        out_specs=[
            pl.BlockSpec((min(OUT_BLOCK, width), width), lambda j: (j, 0)),
            pl.BlockSpec((min(OUT_BLOCK, width), width), lambda j: (j, 0)),
        ],
        out_shape=[out, out],
        scratch_shapes=[pltpu.VMEM((4, width, lanes), jnp.bfloat16)],
        compiler_params=pltpu.CompilerParams(dimension_semantics=("arbitrary",)),
        cost_estimate=pl.CostEstimate(
            flops=2 * 2 * 3 * width * ATOMS * lanes + 4 * 2 * width * width * lanes,
            transcendentals=2 * width * lanes,
            bytes_accessed=2 * width * width * 2 + 3 * ATOMS * lanes * 2 + 2 * width * ATOMS * 2,
        ),
    )(lag, frames, row_signed, col_signed)


def signed_pairs(atom_pairs, first_feature, width):
    first_atoms = lax.dynamic_slice_in_dim(atom_pairs[0], first_feature, width)
    second_atoms = lax.dynamic_slice_in_dim(atom_pairs[1], first_feature, width)
    atom_ids = jnp.arange(ATOMS, dtype=jnp.int32)[None, :]
    return (
        (first_atoms[:, None] == atom_ids).astype(jnp.float32)
        - (second_atoms[:, None] == atom_ids).astype(jnp.float32)
    ).astype(jnp.bfloat16)


def shards(coordinates, resample, block_slot, lag_time, atom_pairs):
    chosen = gather_blocks(coordinates, resample, block_slot)
    width = F // lax.axis_size("row")
    pairs = DRAWS * BLOCK_LEN
    lanes = -(-pairs // 128) * 128
    frames = jnp.transpose(chosen, (2, 3, 0, 1)).reshape(3, ATOMS, pairs)
    frames = jnp.pad(frames, ((0, 0), (0, 0), (0, lanes - pairs)))
    row_signed = signed_pairs(atom_pairs, lax.axis_index("row") * width, width)
    col_signed = signed_pairs(atom_pairs, lax.axis_index("col") * width, width)
    instant, crossed = covariances(lag_time, frames, row_signed, col_signed)
    return (instant[None], crossed[None])


def solution(mesh):
    return jax.shard_map(
        shards,
        mesh=mesh,
        in_specs=(P("rep", None, None, None), P("rep", None), P(), P("rep"), P()),
        out_specs=(P("rep", "row", "col"), P("rep", "row", "col")),
        check_vma=False,
    )
```

```python
import functools

import jax
import jax.numpy as jnp
from jax import lax
from jax.experimental import pallas as pl
from jax.experimental.pallas import tpu as pltpu
from jax.sharding import PartitionSpec as P

F = 4096
ATOMS = 128
BLOCK_LEN = 32
DRAWS = 22
OUT_BLOCK = 1024


def gather_blocks(coordinates, resample, block_slot):
    groups = lax.axis_size("row") * lax.axis_size("col")
    if BLOCK_LEN % groups:
        groups = 1
    frames = BLOCK_LEN // groups
    member = lax.axis_index("row") * lax.axis_size("col") + lax.axis_index("col")
    if groups == 1:
        member = 0
    flat = coordinates.reshape(coordinates.shape[0], BLOCK_LEN, 3 * ATOMS)
    piece = lax.dynamic_slice_in_dim(flat, member * frames, frames, axis=1)
    piece = piece.reshape(piece.shape[0], frames * 3 * ATOMS)
    reps = lax.axis_size("rep")
    spread = jnp.broadcast_to(piece[None], (reps,) + piece.shape)
    every = lax.all_to_all(spread, "rep", 0, 0, tiled=True)
    every = every.reshape(-1, piece.shape[1])
    slots = jnp.take(block_slot, resample[0], axis=0)
    picked = jnp.take(every, slots, axis=0)
    if groups == 1:
        return picked.reshape(DRAWS, BLOCK_LEN, 3, ATOMS)
    spread = jnp.broadcast_to(picked[None], (groups,) + picked.shape)
    parts = lax.all_to_all(spread, ("row", "col"), 0, 0, tiled=True)
    parts = parts.reshape(groups, DRAWS, frames, 3, ATOMS)
    return jnp.swapaxes(parts, 0, 1).reshape(DRAWS, BLOCK_LEN, 3, ATOMS)


def covariance_kernel(lag_ref, x_ref, sr_ref, sc_ref, inst_ref, cross_ref, stack_ref):
    lag = lag_ref[0]
    lanes = x_ref.shape[2]
    count = (2 * DRAWS * (BLOCK_LEN - lag)).astype(jnp.float32)

    @pl.when(pl.program_id(0) == 0)
    def _():
        pair = lax.broadcasted_iota(jnp.int32, (1, lanes), 1)
        first = ((pair % BLOCK_LEN) < (BLOCK_LEN - lag)) & (pair < DRAWS * BLOCK_LEN)

        for tile, signed_ref in enumerate((sr_ref, sc_ref)):
            signed = signed_ref[...]
            total = None
            for c in range(3):
                d = jnp.dot(signed, x_ref[c], preferred_element_type=jnp.float32)
                total = d * d if total is None else total + d * d
            dist = jnp.sqrt(total).astype(jnp.bfloat16).astype(jnp.float32)
            later = pltpu.roll(dist, lanes - lag, 1)
            earlier = jnp.where(first, dist, 0.0)
            later = jnp.where(first, later, 0.0)
            mean = (
                jnp.sum(earlier, axis=1, keepdims=True) + jnp.sum(later, axis=1, keepdims=True)
            ) / count
            stack_ref[2 * tile] = jnp.where(first, earlier - mean, 0.0).astype(jnp.bfloat16)
            stack_ref[2 * tile + 1] = jnp.where(first, later - mean, 0.0).astype(jnp.bfloat16)

    block = inst_ref.shape[0]
    rows = pl.ds(pl.multiple_of(pl.program_id(0) * block, block), block)
    nt = (((1,), (1,)), ((), ()))
    zero_row = stack_ref[0, rows, :]
    lag_row = stack_ref[1, rows, :]
    zero_col = stack_ref[2]
    lag_col = stack_ref[3]
    instant = lax.dot_general(zero_row, zero_col, nt, preferred_element_type=jnp.float32)
    instant = instant + lax.dot_general(lag_row, lag_col, nt, preferred_element_type=jnp.float32)
    inst_ref[...] = (instant / count).astype(inst_ref.dtype)
    crossed = lax.dot_general(zero_row, lag_col, nt, preferred_element_type=jnp.float32)
    crossed = crossed + lax.dot_general(lag_row, zero_col, nt, preferred_element_type=jnp.float32)
    cross_ref[...] = (crossed / count).astype(cross_ref.dtype)


def covariances(lag, frames, row_signed, col_signed):
    lanes = frames.shape[2]
    width = row_signed.shape[0]
    out = jax.ShapeDtypeStruct((width, width), jnp.bfloat16)
    return pl.pallas_call(
        covariance_kernel,
        grid=(pl.cdiv(width, OUT_BLOCK),),
        in_specs=[
            pl.BlockSpec(memory_space=pltpu.SMEM),
            pl.BlockSpec((3, ATOMS, lanes), lambda j: (0, 0, 0)),
            pl.BlockSpec((width, ATOMS), lambda j: (0, 0)),
            pl.BlockSpec((width, ATOMS), lambda j: (0, 0)),
        ],
        out_specs=[
            pl.BlockSpec((min(OUT_BLOCK, width), width), lambda j: (j, 0)),
            pl.BlockSpec((min(OUT_BLOCK, width), width), lambda j: (j, 0)),
        ],
        out_shape=[out, out],
        scratch_shapes=[pltpu.VMEM((4, width, lanes), jnp.bfloat16)],
        compiler_params=pltpu.CompilerParams(dimension_semantics=("arbitrary",)),
        cost_estimate=pl.CostEstimate(
            flops=2 * 2 * 3 * width * ATOMS * lanes + 4 * 2 * width * width * lanes,
            transcendentals=2 * width * lanes,
            bytes_accessed=2 * width * width * 2 + 3 * ATOMS * lanes * 2 + 2 * width * ATOMS * 2,
        ),
    )(lag, frames, row_signed, col_signed)


def signed_pairs(atom_pairs, first_feature, width):
    first_atoms = lax.dynamic_slice_in_dim(atom_pairs[0], first_feature, width)
    second_atoms = lax.dynamic_slice_in_dim(atom_pairs[1], first_feature, width)
    atom_ids = jnp.arange(ATOMS, dtype=jnp.int32)[None, :]
    return (
        (first_atoms[:, None] == atom_ids).astype(jnp.float32)
        - (second_atoms[:, None] == atom_ids).astype(jnp.float32)
    ).astype(jnp.bfloat16)


def shards(coordinates, resample, block_slot, lag_time, atom_pairs):
    chosen = gather_blocks(coordinates, resample, block_slot)
    width = F // lax.axis_size("row")
    pairs = DRAWS * BLOCK_LEN
    lanes = -(-pairs // 128) * 128
    frames = jnp.transpose(chosen, (2, 3, 0, 1)).reshape(3, ATOMS, pairs)
    frames = jnp.pad(frames, ((0, 0), (0, 0), (0, lanes - pairs)))
    row_signed = signed_pairs(atom_pairs, lax.axis_index("row") * width, width)
    col_signed = signed_pairs(atom_pairs, lax.axis_index("col") * width, width)
    instant, crossed = covariances(lag_time, frames, row_signed, col_signed)
    return (instant[None], crossed[None])


def solution(mesh):
    return jax.shard_map(
        shards,
        mesh=mesh,
        in_specs=(P("rep", None, None, None), P("rep", None), P(), P("rep"), P()),
        out_specs=(P("rep", "row", "col"), P("rep", "row", "col")),
        check_vma=False,
    )
```

```python
import functools

import jax
import jax.numpy as jnp
from jax import lax
from jax.experimental import pallas as pl
from jax.experimental.pallas import tpu as pltpu
from jax.sharding import PartitionSpec as P

F = 4096
ATOMS = 128
BLOCK_LEN = 32
DRAWS = 22
OUT_BLOCK = 1024


def gather_blocks(coordinates, resample, block_slot):
    groups = lax.axis_size("row") * lax.axis_size("col")
    if BLOCK_LEN % groups:
        groups = 1
    frames = BLOCK_LEN // groups
    member = lax.axis_index("row") * lax.axis_size("col") + lax.axis_index("col")
    if groups == 1:
        member = 0
    piece = lax.dynamic_slice_in_dim(coordinates, member * frames, frames, axis=1)
    reps = lax.axis_size("rep")
    spread = jnp.broadcast_to(piece[None], (reps,) + piece.shape)
    every = lax.all_to_all(spread, "rep", 0, 0, tiled=True)
    every = every.reshape((-1,) + piece.shape[1:])
    slots = jnp.take(block_slot, resample[0], axis=0)
    picked = jnp.take(every, slots, axis=0)
    if groups == 1:
        return picked
    spread = jnp.broadcast_to(picked[None], (groups,) + picked.shape)
    parts = lax.all_to_all(spread, ("row", "col"), 0, 0, tiled=True)
    return jnp.swapaxes(parts, 0, 1).reshape(DRAWS, BLOCK_LEN, 3, ATOMS)


def covariance_kernel(lag_ref, raw_ref, sr_ref, sc_ref, inst_ref, cross_ref, stack_ref, x_ref):
    lag = lag_ref[0]
    lanes = x_ref.shape[2]
    pairs = raw_ref.shape[2]
    count = (2 * DRAWS * (BLOCK_LEN - lag)).astype(jnp.float32)

    @pl.when(pl.program_id(0) == 0)
    def _():
        x_ref[:, :, pairs:] = jnp.zeros((3, ATOMS, lanes - pairs), x_ref.dtype)
        x_ref[:, :, :pairs] = raw_ref[...]
        pair = lax.broadcasted_iota(jnp.int32, (1, lanes), 1)
        first = ((pair % BLOCK_LEN) < (BLOCK_LEN - lag)) & (pair < DRAWS * BLOCK_LEN)

        for tile, signed_ref in enumerate((sr_ref, sc_ref)):
            signed = signed_ref[...]
            total = None
            for c in range(3):
                d = jnp.dot(signed, x_ref[c], preferred_element_type=jnp.float32)
                total = d * d if total is None else total + d * d
            dist = jnp.sqrt(total).astype(jnp.bfloat16).astype(jnp.float32)
            later = pltpu.roll(dist, lanes - lag, 1)
            earlier = jnp.where(first, dist, 0.0)
            later = jnp.where(first, later, 0.0)
            mean = (
                jnp.sum(earlier, axis=1, keepdims=True) + jnp.sum(later, axis=1, keepdims=True)
            ) / count
            stack_ref[2 * tile] = jnp.where(first, earlier - mean, 0.0).astype(jnp.bfloat16)
            stack_ref[2 * tile + 1] = jnp.where(first, later - mean, 0.0).astype(jnp.bfloat16)

    block = inst_ref.shape[0]
    rows = pl.ds(pl.multiple_of(pl.program_id(0) * block, block), block)
    nt = (((1,), (1,)), ((), ()))
    zero_row = stack_ref[0, rows, :]
    lag_row = stack_ref[1, rows, :]
    zero_col = stack_ref[2]
    lag_col = stack_ref[3]
    instant = lax.dot_general(zero_row, zero_col, nt, preferred_element_type=jnp.float32)
    instant = instant + lax.dot_general(lag_row, lag_col, nt, preferred_element_type=jnp.float32)
    inst_ref[...] = (instant / count).astype(inst_ref.dtype)
    crossed = lax.dot_general(zero_row, lag_col, nt, preferred_element_type=jnp.float32)
    crossed = crossed + lax.dot_general(lag_row, zero_col, nt, preferred_element_type=jnp.float32)
    cross_ref[...] = (crossed / count).astype(cross_ref.dtype)


def covariances(lag, frames, row_signed, col_signed):
    pairs = frames.shape[2]
    lanes = -(-pairs // 128) * 128
    width = row_signed.shape[0]
    out = jax.ShapeDtypeStruct((width, width), jnp.bfloat16)
    return pl.pallas_call(
        covariance_kernel,
        grid=(pl.cdiv(width, OUT_BLOCK),),
        in_specs=[
            pl.BlockSpec(memory_space=pltpu.SMEM),
            pl.BlockSpec((3, ATOMS, pairs), lambda j: (0, 0, 0)),
            pl.BlockSpec((width, ATOMS), lambda j: (0, 0)),
            pl.BlockSpec((width, ATOMS), lambda j: (0, 0)),
        ],
        out_specs=[
            pl.BlockSpec((min(OUT_BLOCK, width), width), lambda j: (j, 0)),
            pl.BlockSpec((min(OUT_BLOCK, width), width), lambda j: (j, 0)),
        ],
        out_shape=[out, out],
        scratch_shapes=[
            pltpu.VMEM((4, width, lanes), jnp.bfloat16),
            pltpu.VMEM((3, ATOMS, lanes), jnp.bfloat16),
        ],
        compiler_params=pltpu.CompilerParams(dimension_semantics=("arbitrary",)),
        cost_estimate=pl.CostEstimate(
            flops=2 * 2 * 3 * width * ATOMS * lanes + 4 * 2 * width * width * lanes,
            transcendentals=2 * width * lanes,
            bytes_accessed=2 * width * width * 2 + 3 * ATOMS * lanes * 2 + 2 * width * ATOMS * 2,
        ),
    )(lag, frames, row_signed, col_signed)


def signed_pairs(atom_pairs, first_feature, width):
    first_atoms = lax.dynamic_slice_in_dim(atom_pairs[0], first_feature, width)
    second_atoms = lax.dynamic_slice_in_dim(atom_pairs[1], first_feature, width)
    atom_ids = jnp.arange(ATOMS, dtype=jnp.int32)[None, :]
    return (
        (first_atoms[:, None] == atom_ids).astype(jnp.float32)
        - (second_atoms[:, None] == atom_ids).astype(jnp.float32)
    ).astype(jnp.bfloat16)


def shards(coordinates, resample, block_slot, lag_time, atom_pairs):
    chosen = gather_blocks(coordinates, resample, block_slot)
    width = F // lax.axis_size("row")
    frames = jnp.transpose(chosen, (2, 3, 0, 1)).reshape(3, ATOMS, DRAWS * BLOCK_LEN)
    row_signed = signed_pairs(atom_pairs, lax.axis_index("row") * width, width)
    col_signed = signed_pairs(atom_pairs, lax.axis_index("col") * width, width)
    instant, crossed = covariances(lag_time, frames, row_signed, col_signed)
    return (instant[None], crossed[None])


def solution(mesh):
    return jax.shard_map(
        shards,
        mesh=mesh,
        in_specs=(P("rep", None, None, None), P("rep", None), P(), P("rep"), P()),
        out_specs=(P("rep", "row", "col"), P("rep", "row", "col")),
        check_vma=False,
    )
```

```python
import functools

import jax
import jax.numpy as jnp
from jax import lax
from jax.experimental import pallas as pl
from jax.experimental.pallas import tpu as pltpu
from jax.sharding import PartitionSpec as P

F = 4096
ATOMS = 128
BLOCK_LEN = 32
DRAWS = 22
OUT_BLOCK = 1024


def gather_blocks(coordinates, resample, block_slot):
    groups = lax.axis_size("row") * lax.axis_size("col")
    if BLOCK_LEN % groups:
        groups = 1
    frames = BLOCK_LEN // groups
    member = lax.axis_index("row") * lax.axis_size("col") + lax.axis_index("col")
    if groups == 1:
        member = 0
    flat = coordinates.reshape(coordinates.shape[0], BLOCK_LEN, 3 * ATOMS)
    piece = lax.dynamic_slice_in_dim(flat, member * frames, frames, axis=1)
    piece = piece.reshape(piece.shape[0], -1)
    every = lax.all_gather(piece, "rep", axis=0, tiled=True)
    every = every.reshape(-1, frames, 3, ATOMS)
    slots = jnp.take(block_slot, resample[0], axis=0)
    picked = jnp.take(every, slots, axis=0)
    if groups == 1:
        return picked
    spread = jnp.broadcast_to(picked[None], (groups,) + picked.shape)
    parts = lax.all_to_all(spread, ("row", "col"), 0, 0, tiled=True)
    return jnp.swapaxes(parts, 0, 1).reshape(DRAWS, BLOCK_LEN, 3, ATOMS)


def covariance_kernel(lag_ref, x_ref, sr_ref, sc_ref, inst_ref, cross_ref, stack_ref):
    lag = lag_ref[0]
    lanes = x_ref.shape[2]
    count = (2 * DRAWS * (BLOCK_LEN - lag)).astype(jnp.float32)

    @pl.when(pl.program_id(0) == 0)
    def _():
        pair = lax.broadcasted_iota(jnp.int32, (1, lanes), 1)
        first = ((pair % BLOCK_LEN) < (BLOCK_LEN - lag)) & (pair < DRAWS * BLOCK_LEN)

        for tile, signed_ref in enumerate((sr_ref, sc_ref)):
            signed = signed_ref[...]
            total = None
            for c in range(3):
                d = jnp.dot(signed, x_ref[c], preferred_element_type=jnp.float32)
                total = d * d if total is None else total + d * d
            dist = jnp.sqrt(total).astype(jnp.bfloat16).astype(jnp.float32)
            later = pltpu.roll(dist, lanes - lag, 1)
            earlier = jnp.where(first, dist, 0.0)
            later = jnp.where(first, later, 0.0)
            mean = (
                jnp.sum(earlier, axis=1, keepdims=True) + jnp.sum(later, axis=1, keepdims=True)
            ) / count
            stack_ref[2 * tile] = jnp.where(first, earlier - mean, 0.0).astype(jnp.bfloat16)
            stack_ref[2 * tile + 1] = jnp.where(first, later - mean, 0.0).astype(jnp.bfloat16)

    block = inst_ref.shape[0]
    rows = pl.ds(pl.multiple_of(pl.program_id(0) * block, block), block)
    nt = (((1,), (1,)), ((), ()))
    zero_row = stack_ref[0, rows, :]
    lag_row = stack_ref[1, rows, :]
    zero_col = stack_ref[2]
    lag_col = stack_ref[3]
    instant = lax.dot_general(zero_row, zero_col, nt, preferred_element_type=jnp.float32)
    instant = instant + lax.dot_general(lag_row, lag_col, nt, preferred_element_type=jnp.float32)
    inst_ref[...] = (instant / count).astype(inst_ref.dtype)
    crossed = lax.dot_general(zero_row, lag_col, nt, preferred_element_type=jnp.float32)
    crossed = crossed + lax.dot_general(lag_row, zero_col, nt, preferred_element_type=jnp.float32)
    cross_ref[...] = (crossed / count).astype(cross_ref.dtype)


def covariances(lag, frames, row_signed, col_signed):
    lanes = frames.shape[2]
    width = row_signed.shape[0]
    out = jax.ShapeDtypeStruct((width, width), jnp.bfloat16)
    return pl.pallas_call(
        covariance_kernel,
        grid=(pl.cdiv(width, OUT_BLOCK),),
        in_specs=[
            pl.BlockSpec(memory_space=pltpu.SMEM),
            pl.BlockSpec((3, ATOMS, lanes), lambda j: (0, 0, 0)),
            pl.BlockSpec((width, ATOMS), lambda j: (0, 0)),
            pl.BlockSpec((width, ATOMS), lambda j: (0, 0)),
        ],
        out_specs=[
            pl.BlockSpec((min(OUT_BLOCK, width), width), lambda j: (j, 0)),
            pl.BlockSpec((min(OUT_BLOCK, width), width), lambda j: (j, 0)),
        ],
        out_shape=[out, out],
        scratch_shapes=[pltpu.VMEM((4, width, lanes), jnp.bfloat16)],
        compiler_params=pltpu.CompilerParams(dimension_semantics=("arbitrary",)),
        cost_estimate=pl.CostEstimate(
            flops=2 * 2 * 3 * width * ATOMS * lanes + 4 * 2 * width * width * lanes,
            transcendentals=2 * width * lanes,
            bytes_accessed=2 * width * width * 2 + 3 * ATOMS * lanes * 2 + 2 * width * ATOMS * 2,
        ),
    )(lag, frames, row_signed, col_signed)


def signed_pairs(atom_pairs, first_feature, width):
    first_atoms = lax.dynamic_slice_in_dim(atom_pairs[0], first_feature, width)
    second_atoms = lax.dynamic_slice_in_dim(atom_pairs[1], first_feature, width)
    atom_ids = jnp.arange(ATOMS, dtype=jnp.int32)[None, :]
    return (
        (first_atoms[:, None] == atom_ids).astype(jnp.float32)
        - (second_atoms[:, None] == atom_ids).astype(jnp.float32)
    ).astype(jnp.bfloat16)


def shards(coordinates, resample, block_slot, lag_time, atom_pairs):
    chosen = gather_blocks(coordinates, resample, block_slot)
    width = F // lax.axis_size("row")
    pairs = DRAWS * BLOCK_LEN
    lanes = -(-pairs // 128) * 128
    frames = jnp.transpose(chosen, (2, 3, 0, 1)).reshape(3, ATOMS, pairs)
    frames = jnp.pad(frames, ((0, 0), (0, 0), (0, lanes - pairs)))
    row_signed = signed_pairs(atom_pairs, lax.axis_index("row") * width, width)
    col_signed = signed_pairs(atom_pairs, lax.axis_index("col") * width, width)
    instant, crossed = covariances(lag_time, frames, row_signed, col_signed)
    return (instant[None], crossed[None])


def solution(mesh):
    return jax.shard_map(
        shards,
        mesh=mesh,
        in_specs=(P("rep", None, None, None), P("rep", None), P(), P("rep"), P()),
        out_specs=(P("rep", "row", "col"), P("rep", "row", "col")),
        check_vma=False,
    )
```

```python
import functools

import jax
import jax.numpy as jnp
from jax import lax
from jax.experimental import pallas as pl
from jax.experimental.pallas import tpu as pltpu
from jax.sharding import PartitionSpec as P

F = 4096
ATOMS = 128
BLOCK_LEN = 32
DRAWS = 22
OUT_BLOCK = 1024


def gather_blocks(coordinates, resample, block_slot):
    groups = lax.axis_size("row") * lax.axis_size("col")
    if BLOCK_LEN % groups:
        groups = 1
    frames = BLOCK_LEN // groups
    member = lax.axis_index("row") * lax.axis_size("col") + lax.axis_index("col")
    if groups == 1:
        member = 0
    piece = lax.dynamic_slice_in_dim(coordinates, member * frames, frames, axis=1)
    reps = lax.axis_size("rep")
    spread = jnp.broadcast_to(piece[None], (reps,) + piece.shape)
    every = lax.all_to_all(spread, "rep", 0, 0, tiled=True)
    every = every.reshape((-1,) + piece.shape[1:])
    slots = jnp.take(block_slot, resample[0], axis=0)
    picked = jnp.take(every, slots, axis=0)
    if groups == 1:
        return picked
    spread = jnp.broadcast_to(picked[None], (groups,) + picked.shape)
    parts = lax.all_to_all(spread, ("row", "col"), 0, 0, tiled=True)
    return jnp.swapaxes(parts, 0, 1).reshape(DRAWS, BLOCK_LEN, 3, ATOMS)


def covariance_kernel(lag_ref, x_ref, sr_ref, sc_ref, inst_ref, cross_ref, stack_ref):
    lag = lag_ref[0]
    lanes = x_ref.shape[2]
    count = (2 * DRAWS * (BLOCK_LEN - lag)).astype(jnp.float32)

    @pl.when(pl.program_id(0) == 0)
    def _():
        pair = lax.broadcasted_iota(jnp.int32, (1, lanes), 1)
        first = ((pair % BLOCK_LEN) < (BLOCK_LEN - lag)) & (pair < DRAWS * BLOCK_LEN)

        for tile, signed_ref in enumerate((sr_ref, sc_ref)):
            signed = signed_ref[...]
            total = None
            for c in range(3):
                d = jnp.dot(signed, x_ref[c], preferred_element_type=jnp.float32)
                total = d * d if total is None else total + d * d
            dist = jnp.sqrt(total).astype(jnp.bfloat16).astype(jnp.float32)
            later = pltpu.roll(dist, lanes - lag, 1)
            earlier = jnp.where(first, dist, 0.0)
            later = jnp.where(first, later, 0.0)
            mean = (
                jnp.sum(earlier, axis=1, keepdims=True) + jnp.sum(later, axis=1, keepdims=True)
            ) / count
            zero_lag = jnp.where(first, earlier - mean, 0.0).astype(jnp.bfloat16)
            lagged = jnp.where(first, later - mean, 0.0).astype(jnp.bfloat16)
            stack_ref[tile, :, :lanes] = zero_lag
            stack_ref[tile, :, lanes:] = lagged
            if tile == 1:
                stack_ref[2, :, :lanes] = lagged
                stack_ref[2, :, lanes:] = zero_lag

    block = inst_ref.shape[0]
    rows = pl.ds(pl.multiple_of(pl.program_id(0) * block, block), block)
    nt = (((1,), (1,)), ((), ()))
    stacked = stack_ref[0, rows, :]
    instant = lax.dot_general(stacked, stack_ref[1], nt, preferred_element_type=jnp.float32)
    inst_ref[...] = (instant / count).astype(inst_ref.dtype)
    crossed = lax.dot_general(stacked, stack_ref[2], nt, preferred_element_type=jnp.float32)
    cross_ref[...] = (crossed / count).astype(cross_ref.dtype)


def covariances(lag, frames, row_signed, col_signed):
    lanes = frames.shape[2]
    width = row_signed.shape[0]
    out = jax.ShapeDtypeStruct((width, width), jnp.bfloat16)
    return pl.pallas_call(
        covariance_kernel,
        grid=(pl.cdiv(width, OUT_BLOCK),),
        in_specs=[
            pl.BlockSpec(memory_space=pltpu.SMEM),
            pl.BlockSpec((3, ATOMS, lanes), lambda j: (0, 0, 0)),
            pl.BlockSpec((width, ATOMS), lambda j: (0, 0)),
            pl.BlockSpec((width, ATOMS), lambda j: (0, 0)),
        ],
        out_specs=[
            pl.BlockSpec((min(OUT_BLOCK, width), width), lambda j: (j, 0)),
            pl.BlockSpec((min(OUT_BLOCK, width), width), lambda j: (j, 0)),
        ],
        out_shape=[out, out],
        scratch_shapes=[pltpu.VMEM((3, width, 2 * lanes), jnp.bfloat16)],
        compiler_params=pltpu.CompilerParams(dimension_semantics=("arbitrary",)),
        cost_estimate=pl.CostEstimate(
            flops=2 * 2 * 3 * width * ATOMS * lanes + 4 * 2 * width * width * lanes,
            transcendentals=2 * width * lanes,
            bytes_accessed=2 * width * width * 2 + 3 * ATOMS * lanes * 2 + 2 * width * ATOMS * 2,
        ),
    )(lag, frames, row_signed, col_signed)


def signed_pairs(atom_pairs, first_feature, width):
    first_atoms = lax.dynamic_slice_in_dim(atom_pairs[0], first_feature, width)
    second_atoms = lax.dynamic_slice_in_dim(atom_pairs[1], first_feature, width)
    atom_ids = jnp.arange(ATOMS, dtype=jnp.int32)[None, :]
    return (
        (first_atoms[:, None] == atom_ids).astype(jnp.float32)
        - (second_atoms[:, None] == atom_ids).astype(jnp.float32)
    ).astype(jnp.bfloat16)


def shards(coordinates, resample, block_slot, lag_time, atom_pairs):
    chosen = gather_blocks(coordinates, resample, block_slot)
    width = F // lax.axis_size("row")
    pairs = DRAWS * BLOCK_LEN
    lanes = -(-pairs // 128) * 128
    frames = jnp.transpose(chosen, (2, 3, 0, 1)).reshape(3, ATOMS, pairs)
    frames = jnp.pad(frames, ((0, 0), (0, 0), (0, lanes - pairs)))
    row_signed = signed_pairs(atom_pairs, lax.axis_index("row") * width, width)
    col_signed = signed_pairs(atom_pairs, lax.axis_index("col") * width, width)
    instant, crossed = covariances(lag_time, frames, row_signed, col_signed)
    return (instant[None], crossed[None])


def solution(mesh):
    return jax.shard_map(
        shards,
        mesh=mesh,
        in_specs=(P("rep", None, None, None), P("rep", None), P(), P("rep"), P()),
        out_specs=(P("rep", "row", "col"), P("rep", "row", "col")),
        check_vma=False,
    )
```
